256 devices in a mesh: seq: 32 (over z, y_lo, core), tp: 8 (over y_hi, x).
Axes of the slice: x: 4, y: 4 (y_hi: 2, y_lo: 2; y = y_hi * 2 + y_lo), z: 8, core: 2. Of those that a mesh axis runs over, the one named last changes fastest.
Arguments:
- qkv_se: bfloat16 [16384, 3, 4096], P('seq', None, 'tp'), may hold values from -6 to 6
- residual: bfloat16 [16384, 4096], P('seq', 'tp'), may hold values from -108 to 108
- taps_se: bfloat16 [256, 7], P('tp'), may hold values from -2 to 2
- skip_se: bfloat16 [4096], P('tp'), may hold values from 0.5 to 1.5
- w_out: bfloat16 [4096, 4096], P('tp', 'seq'), may hold values from -0.1875 to 0.1875
- norm_gain: bfloat16 [4096], replicated, may hold values from 0.5 to 1.5
- w_in: bfloat16 [4096, 3, 4096], P('seq', None, 'tp'), may hold values from -0.09375 to 0.09375
- taps_mr: bfloat16 [256, 128], P('tp'), may hold values from -0.5 to 0.5
- skip_mr: bfloat16 [4096], P('tp'), may hold values from 0.5 to 1.5
Outputs:
- mixed: bfloat16 [16384, 4096], P('seq', 'tp')
The draws below stay inside these ranges and needn't reach their ends.
All inputs are finite; a program needn't handle non-finite values.
Results may differ from the reference program's by a relative error of at most 0.0085.
Values may be sent and summed in bfloat16 or wider, within the bound.
No kernel may reach another device: no remote copies, remote signals or barrier semaphores. Data moves between devices by JAX's collectives and lax.ppermute only.
A program may use at most 64 MiB of HBM per device.

```python
import math
import jax
import jax.numpy as jnp
from jax import lax

D = 4096
GROUP = 16
SE_TAPS = 7
MR_TAPS = 128
TOKENS = 16384
GROUPS = 256


def draw_residual(key, part):
    key_base, key_rows, key_cols = jax.random.split(key, 3)
    row_scale = jnp.exp(jax.random.uniform(key_rows, (TOKENS, 1), jnp.float32, math.log(0.3), math.log(3.0)))
    column_index = jnp.arange(D, dtype=jnp.float32)[None, :] / D
    col_scale = jnp.exp(jax.random.uniform(key_cols, (1, D), jnp.float32, math.log(0.5), math.log(2.0)))
    col_scale = col_scale * jnp.exp(math.log(3.0) * column_index)
    base = jnp.clip(jax.random.normal(key_base, (TOKENS, D), jnp.float32), -6.0, 6.0)
    return (base * row_scale * col_scale).astype(jnp.bfloat16)


def spiked(drawn, own_key, source, target, blocks, factor):
    def block_of(position):
        return (jnp.arange(drawn.shape[position]) // (drawn.shape[position] // blocks)).reshape((-1,) + (1,) * (drawn.ndim - 1 - position))

    one_side = jax.random.permutation(own_key, blocks)[block_of(target)]
    other_side = (block_of(target) + blocks // 2) % blocks
    return jnp.where((block_of(source) == one_side) | (block_of(source) == other_side), factor * drawn, drawn)


def steps_of(stream_key, dims, cuts, least, top_value):
    loudness, own = 1.0, jax.random.fold_in(stream_key, 6)
    for position, shards_of in cuts:
        draws = jnp.exp(jax.random.uniform(jax.random.fold_in(own, position), (shards_of,), jnp.float32, least / len(cuts), top_value / len(cuts)))
        loudness = loudness * jnp.repeat(draws, dims[position] // shards_of).reshape([-1 if axis == position else 1 for axis in range(len(dims))])
    return loudness


def scatter_about(rng, extent, deviation, most, shards=(), kind=jnp.bfloat16):
    array = jax.random.normal(rng, extent, jnp.float32) * deviation
    if len(shards) > 0:
        array = steps_of(rng, extent, shards, -0.22, 0.18) * array
    return jnp.clip(array, min=-most, max=most).astype(kind)


def gaussian_with(own_key, dims, deviation, bound, pieces, heavy, held_as=jnp.bfloat16):
    array = deviation * jax.random.normal(own_key, dims, jnp.float32)
    if pieces:
        array = array * steps_of(own_key, dims, pieces, -0.22, 0.18)
    return jnp.clip(spiked(array, jax.random.fold_in(own_key, 3), *heavy), -bound, bound).astype(held_as)


def setup_inputs(seed: int = 0) -> dict:
    seeds = jax.random.split(jax.random.key(seed), 10)
    return {
        "qkv_se": scatter_about(seeds[0], (TOKENS, 3, D), 1.0, 6.0, ((0, 32), (2, 8))),
        "residual": draw_residual(jax.random.fold_in(seeds[9], 71), 0),
        "taps_se": scatter_about(seeds[2], (GROUPS, SE_TAPS), SE_TAPS ** -0.5, 2.0, ((0, 8),)),
        "skip_se": jnp.clip(0.5 + 1.0 * jax.random.uniform(seeds[3], (D,), jnp.float32) ** steps_of(seeds[3], (D,), ((0, 8),), -0.2, 0.2), 0.5, 1.5).astype(jnp.bfloat16),
        "w_out": gaussian_with(seeds[4], (D, D), D ** -0.5, 0.1875, ((0, 8), (1, 32)), (0, 1, 32, 2.75)),
        "norm_gain": jnp.clip(1.0 + 0.1 * jax.random.normal(seeds[5], (D,), jnp.float32), 0.5, 1.5).astype(jnp.bfloat16),
        "w_in": scatter_about(seeds[6], (D, 3, D), D ** -0.5, 0.09375, ((0, 32), (2, 8))),
        "taps_mr": scatter_about(seeds[7], (GROUPS, MR_TAPS), MR_TAPS ** -0.5, 0.5, ((0, 8),)),
        "skip_mr": jnp.clip(0.5 + 1.0 * jax.random.uniform(seeds[8], (D,), jnp.float32) ** steps_of(seeds[8], (D,), ((0, 8),), -0.2, 0.2), 0.5, 1.5).astype(jnp.bfloat16),
    }


norm_eps = 1e-05

def short_conv(values, taps):
    per_channel = jnp.repeat(taps.astype(jnp.float32), GROUP, axis=0)
    wide = values.astype(jnp.float32)
    padded = jnp.concatenate([jnp.zeros((SE_TAPS - 1, wide.shape[1]), jnp.float32), wide], axis=0)
    total = jnp.zeros_like(wide)
    for tap_index in range(SE_TAPS):
        begin = SE_TAPS - 1 - tap_index
        total = total + per_channel[:, tap_index] * padded[begin:begin + wide.shape[0]]
    return total

def toeplitz_pair(taps):
    offsets = jnp.arange(MR_TAPS)[:, None] - jnp.arange(MR_TAPS)[None, :]
    table = taps[:, jnp.remainder(offsets, MR_TAPS)]
    lower = jnp.where(offsets >= 0, table, jnp.zeros_like(table))
    upper = jnp.where(offsets < 0, table, jnp.zeros_like(table))
    return (lower, upper)

def long_conv(values, taps):
    count = values.shape[0]
    chans = values.shape[1]
    lower, upper = toeplitz_pair(taps.astype(jnp.float32))
    blocks = values.astype(jnp.float32).reshape(count // MR_TAPS, MR_TAPS, chans // GROUP, GROUP)
    earlier = jnp.concatenate([jnp.zeros_like(blocks[:1]), blocks[:-1]], axis=0)
    result = jnp.einsum('gts,bsgc->btgc', lower, blocks) + jnp.einsum('gts,bsgc->btgc', upper, earlier)
    return result.reshape(count, chans)

def reference(qkv_se, residual, taps_se, skip_se, w_out, norm_gain, w_in, taps_mr, skip_mr):
    query_se = qkv_se[:, 0].astype(jnp.float32)
    u_se = (qkv_se[:, 1].astype(jnp.float32) * qkv_se[:, 2].astype(jnp.float32)).astype(jnp.bfloat16)
    conv_se = short_conv(u_se, taps_se)
    y_se = (query_se * (conv_se + skip_se.astype(jnp.float32) * u_se.astype(jnp.float32))).astype(jnp.bfloat16)
    stream = residual.astype(jnp.float32) + jnp.dot(y_se, w_out, preferred_element_type=jnp.float32)
    scale = lax.rsqrt(lax.optimization_barrier(jnp.mean(stream * stream, axis=1, keepdims=True)) + norm_eps)
    normed = (stream * scale * norm_gain.astype(jnp.float32)).astype(jnp.bfloat16)
    proj = jnp.dot(normed, w_in.reshape(D, 3 * D), preferred_element_type=jnp.float32).reshape(TOKENS, 3, D)
    query_mr = proj[:, 0]
    u_mr = (proj[:, 1] * proj[:, 2]).astype(jnp.bfloat16)
    conv_mr = long_conv(u_mr, taps_mr)
    return (query_mr * (conv_mr + skip_mr.astype(jnp.float32) * u_mr.astype(jnp.float32))).astype(jnp.bfloat16)
```

```python
import jax
import jax.numpy as jnp
from jax import lax
from jax.sharding import PartitionSpec as P

GROUP = 16
SE_TAPS = 7
MR_TAPS = 128


norm_eps = 1e-05


def shifted(block, axis, distance):
    devices = range(lax.axis_size(axis))
    route = [(i - distance, i) for i in devices if i - distance in devices]
    return lax.ppermute(block, axis, route)


def toeplitz_pair(taps):
    offsets = lax.broadcasted_iota(jnp.int32, (MR_TAPS, MR_TAPS), 0) - lax.broadcasted_iota(
        jnp.int32, (MR_TAPS, MR_TAPS), 1
    )
    lag_ids = lax.broadcasted_iota(jnp.int32, (MR_TAPS, MR_TAPS, MR_TAPS), 0)
    picks = (jnp.remainder(offsets, MR_TAPS)[None] == lag_ids).astype(jnp.bfloat16)
    table = jnp.einsum("gj,jts->gts", taps, picks, preferred_element_type=jnp.float32).astype(
        jnp.bfloat16
    )
    lower = jnp.where(offsets[None] >= 0, table, jnp.zeros_like(table))
    upper = jnp.where(offsets[None] < 0, table, jnp.zeros_like(table))
    return (lower, upper)


def project_out(y_se, w_out):
    tp_size = lax.axis_size("tp")
    stacked = lax.all_gather(w_out, "seq", axis=0, tiled=False)
    per_tp = stacked.reshape(tp_size, stacked.shape[0] // tp_size, *stacked.shape[1:])
    partial = jnp.einsum("tc,kjcf->ktjf", y_se, per_tp, preferred_element_type=jnp.float32)
    return partial.reshape(tp_size, y_se.shape[0], -1)


def per_device(qkv_se, residual, taps_se, skip_se, w_out, norm_gain, w_in, taps_mr, skip_mr):
    row_count = qkv_se.shape[0]
    chan_width = qkv_se.shape[2]
    local_groups = chan_width // GROUP
    query_se = qkv_se[:, 0].astype(jnp.float32)
    u_se = (qkv_se[:, 1].astype(jnp.float32) * qkv_se[:, 2].astype(jnp.float32)).astype(
        jnp.bfloat16
    )
    incoming_se = shifted(u_se[row_count - (SE_TAPS - 1) :], "seq", 1)
    extended = jnp.concatenate([incoming_se, u_se], axis=0).astype(jnp.float32)
    per_channel = jnp.repeat(taps_se.astype(jnp.float32), GROUP, axis=0)
    conv_se = jnp.zeros((row_count, chan_width), jnp.float32)
    for tap_index in range(SE_TAPS):
        begin = SE_TAPS - 1 - tap_index
        conv_se = conv_se + per_channel[:, tap_index] * extended[begin : begin + row_count]
    y_se = (query_se * (conv_se + skip_se.astype(jnp.float32) * u_se.astype(jnp.float32))).astype(
        jnp.bfloat16
    )
    gain_full = norm_gain.astype(jnp.float32)
    partial_out = project_out(y_se, w_out)
    share = lax.psum_scatter(partial_out, "tp", scatter_dimension=0, tiled=True)[0]
    stream = residual.astype(jnp.float32) + share
    squares = lax.psum(jnp.sum(stream * stream, axis=1), "tp")
    scale = lax.rsqrt(squares / (chan_width * lax.axis_size("tp")) + norm_eps)
    my_gain = lax.dynamic_slice_in_dim(gain_full, lax.axis_index("tp") * chan_width, chan_width, 0)
    normed = (stream * scale[:, None] * my_gain).astype(jnp.bfloat16)
    gathered = lax.all_gather(normed, "tp", axis=0, tiled=False)
    piece = lax.all_gather(w_in, "seq", axis=0, tiled=True)
    flat_piece = piece.reshape(gathered.shape[0], chan_width, 3 * chan_width)
    proj = jnp.einsum(
        "ktf,kfn->tn", gathered, flat_piece, preferred_element_type=jnp.float32
    ).reshape(row_count, 3, chan_width)
    query_mr = proj[:, 0]
    u_mr = (proj[:, 1] * proj[:, 2]).astype(jnp.bfloat16)
    lower, upper = toeplitz_pair(taps_mr)
    block_count = row_count // MR_TAPS
    blocks = u_mr.reshape(block_count, MR_TAPS, local_groups, GROUP)
    inside = jnp.einsum("gts,bsgc->btgc", lower, blocks, preferred_element_type=jnp.float32)
    tail_rows = shifted(blocks[block_count - 1], "seq", 1)
    earlier = jnp.concatenate([tail_rows[None], blocks[: block_count - 1]], axis=0)
    conv_mr = inside + jnp.einsum(
        "gts,bsgc->btgc", upper, earlier, preferred_element_type=jnp.float32
    )
    conv_mr = conv_mr.reshape(row_count, chan_width)
    return (query_mr * (conv_mr + skip_mr.astype(jnp.float32) * u_mr.astype(jnp.float32))).astype(
        jnp.bfloat16
    )


def solution(mesh):
    placed = (
        P("seq", None, "tp"),
        P("seq", "tp"),
        P("tp", None),
        P("tp"),
        P("tp", "seq"),
        P(),
        P("seq", None, "tp"),
        P("tp", None),
        P("tp"),
    )
    return jax.shard_map(
        per_device, mesh=mesh, in_specs=placed, out_specs=P("seq", "tp"), check_vma=False
    )
```

```python
import jax
import jax.numpy as jnp
from jax import lax
from jax.sharding import PartitionSpec as P

GROUP = 16
SE_TAPS = 7
MR_TAPS = 128


norm_eps = 1e-05


def shifted(block, axis, distance):
    devices = range(lax.axis_size(axis))
    route = [(i - distance, i) for i in devices if i - distance in devices]
    return lax.ppermute(block, axis, route)


def seq_coords(index):
    return index // 4, (index // 2) % 2, index % 2


def seq_of(z, y_lo, core):
    return z * 4 + y_lo * 2 + core


def exchange(block, axis, pairs):
    return lax.ppermute(block, axis, pairs)


def gather_rows(piece):
    seq_size = lax.axis_size("seq")
    z_size = seq_size // 4
    me = lax.axis_index("seq")
    other = exchange(piece, "seq", [(i, i ^ 2) for i in range(seq_size)])
    mine_first = (me // 2) % 2 == 0
    block = jnp.stack(
        [jnp.where(mine_first, piece, other), jnp.where(mine_first, other, piece)]
    )
    ahead = []
    behind = []
    for i in range(seq_size):
        z, y_lo, core = seq_coords(i)
        ahead.append((i, seq_of((z + 1) % z_size, y_lo, core)))
        behind.append((i, seq_of((z - 1) % z_size, y_lo, core)))
    core_pair = [(i, i ^ 1) for i in range(seq_size)]
    blocks = [(0, block)]
    moving_up = block
    moving_down = block
    for step in range(1, z_size // 2 + 1):
        moving_up = exchange(moving_up, "seq", ahead)
        blocks.append((step, moving_up))
        if step < z_size // 2:
            moving_down = exchange(moving_down, "seq", behind)
            blocks.append((z_size - step, moving_down))
    return [(k, mine, exchange(mine, "seq", core_pair)) for k, mine in blocks]


def project_in(gathered, pieces, rows):
    seq_size = lax.axis_size("seq")
    z_size = seq_size // 4
    me = lax.axis_index("seq")
    my_z = me // 4
    my_core = me % 2
    features = gathered.reshape(z_size, gathered.shape[1], 2, 2, rows)
    total = None
    for k, mine, partner in pieces:
        z_k = (my_z - k) % z_size
        for core, weights in ((my_core, mine), (1 - my_core, partner)):
            lhs = lax.dynamic_slice(
                features, (z_k, 0, 0, core, 0), (1, features.shape[1], 2, 1, rows)
            ).reshape(features.shape[1], 2, rows)
            part = jnp.einsum("tyr,yrin->tin", lhs, weights, preferred_element_type=jnp.float32)
            total = part if total is None else total + part
    return total


def tp_sum(value):
    tp_size = lax.axis_size("tp")
    total = value
    bit = 1
    while bit < tp_size:
        total = total + lax.ppermute(total, "tp", [(i, i ^ bit) for i in range(tp_size)])
        bit *= 2
    return total


def toeplitz_pair(taps):
    offsets = lax.broadcasted_iota(jnp.int32, (MR_TAPS, MR_TAPS), 0) - lax.broadcasted_iota(
        jnp.int32, (MR_TAPS, MR_TAPS), 1
    )
    lag_ids = lax.broadcasted_iota(jnp.int32, (MR_TAPS, MR_TAPS, MR_TAPS), 0)
    picks = (jnp.remainder(offsets, MR_TAPS)[None] == lag_ids).astype(jnp.bfloat16)
    table = jnp.einsum("gj,jts->gts", taps, picks, preferred_element_type=jnp.float32).astype(
        jnp.bfloat16
    )
    lower = jnp.where(offsets[None] >= 0, table, jnp.zeros_like(table))
    upper = jnp.where(offsets[None] < 0, table, jnp.zeros_like(table))
    return (lower, upper)


def project_out(y_se, w_out):
    tp_size = lax.axis_size("tp")
    stacked = lax.all_gather(w_out, "seq", axis=0, tiled=False)
    per_tp = stacked.reshape(tp_size, stacked.shape[0] // tp_size, *stacked.shape[1:])
    partial = jnp.einsum("tc,kjcf->ktjf", y_se, per_tp, preferred_element_type=jnp.float32)
    return partial.reshape(tp_size, y_se.shape[0], -1)


def per_device(qkv_se, residual, taps_se, skip_se, w_out, norm_gain, w_in, taps_mr, skip_mr):
    row_count = qkv_se.shape[0]
    chan_width = qkv_se.shape[2]
    local_groups = chan_width // GROUP
    query_se = qkv_se[:, 0].astype(jnp.float32)
    u_se = (qkv_se[:, 1].astype(jnp.float32) * qkv_se[:, 2].astype(jnp.float32)).astype(
        jnp.bfloat16
    )
    incoming_se = shifted(u_se[row_count - (SE_TAPS - 1) :], "seq", 1)
    extended = jnp.concatenate([incoming_se, u_se], axis=0).astype(jnp.float32)
    per_channel = jnp.repeat(taps_se.astype(jnp.float32), GROUP, axis=0)
    conv_se = jnp.zeros((row_count, chan_width), jnp.float32)
    for tap_index in range(SE_TAPS):
        begin = SE_TAPS - 1 - tap_index
        conv_se = conv_se + per_channel[:, tap_index] * extended[begin : begin + row_count]
    y_se = (query_se * (conv_se + skip_se.astype(jnp.float32) * u_se.astype(jnp.float32))).astype(
        jnp.bfloat16
    )
    gain_full = norm_gain.astype(jnp.float32)
    partial_out = project_out(y_se, w_out)
    share = lax.psum_scatter(partial_out, "tp", scatter_dimension=0, tiled=True)[0]
    pieces = gather_rows(w_in)
    share, pieces = lax.optimization_barrier((share, pieces))
    stream = residual.astype(jnp.float32) + share
    squares = tp_sum(jnp.sum(stream * stream, axis=1))
    scale = lax.rsqrt(squares / (chan_width * lax.axis_size("tp")) + norm_eps)
    my_gain = lax.dynamic_slice_in_dim(gain_full, lax.axis_index("tp") * chan_width, chan_width, 0)
    normed = (stream * scale[:, None] * my_gain).astype(jnp.bfloat16)
    gathered = lax.all_gather(normed, "tp", axis=0, tiled=False)
    proj = project_in(gathered, pieces, w_in.shape[0])
    query_mr = proj[:, 0]
    u_mr = (proj[:, 1] * proj[:, 2]).astype(jnp.bfloat16)
    lower, upper = toeplitz_pair(taps_mr)
    block_count = row_count // MR_TAPS
    blocks = u_mr.reshape(block_count, MR_TAPS, local_groups, GROUP)
    inside = jnp.einsum("gts,bsgc->btgc", lower, blocks, preferred_element_type=jnp.float32)
    tail_rows = shifted(blocks[block_count - 1], "seq", 1)
    earlier = jnp.concatenate([tail_rows[None], blocks[: block_count - 1]], axis=0)
    conv_mr = inside + jnp.einsum(
        "gts,bsgc->btgc", upper, earlier, preferred_element_type=jnp.float32
    )
    conv_mr = conv_mr.reshape(row_count, chan_width)
    return (query_mr * (conv_mr + skip_mr.astype(jnp.float32) * u_mr.astype(jnp.float32))).astype(
        jnp.bfloat16
    )


def solution(mesh):
    placed = (
        P("seq", None, "tp"),
        P("seq", "tp"),
        P("tp", None),
        P("tp"),
        P("tp", "seq"),
        P(),
        P("seq", None, "tp"),
        P("tp", None),
        P("tp"),
    )
    return jax.shard_map(
        per_device, mesh=mesh, in_specs=placed, out_specs=P("seq", "tp"), check_vma=False
    )
```

```python
import jax
import jax.numpy as jnp
from jax import lax
from jax.sharding import PartitionSpec as P

GROUP = 16
SE_TAPS = 7
MR_TAPS = 128


norm_eps = 1e-05


def shifted(block, axis, distance):
    devices = range(lax.axis_size(axis))
    route = [(i - distance, i) for i in devices if i - distance in devices]
    return lax.ppermute(block, axis, route)


def seq_coords(index):
    return index // 4, (index // 2) % 2, index % 2


def seq_of(z, y_lo, core):
    return z * 4 + y_lo * 2 + core


def exchange(block, axis, pairs):
    return lax.ppermute(block, axis, pairs)


def gather_rows(piece):
    seq_size = lax.axis_size("seq")
    z_size = seq_size // 4
    me = lax.axis_index("seq")
    other = exchange(piece, "seq", [(i, i ^ 2) for i in range(seq_size)])
    mine_first = (me // 2) % 2 == 0
    block = jnp.stack(
        [jnp.where(mine_first, piece, other), jnp.where(mine_first, other, piece)]
    )
    ahead = []
    behind = []
    for i in range(seq_size):
        z, y_lo, core = seq_coords(i)
        ahead.append((i, seq_of((z + 1) % z_size, y_lo, core)))
        behind.append((i, seq_of((z - 1) % z_size, y_lo, core)))
    core_pair = [(i, i ^ 1) for i in range(seq_size)]
    blocks = [(0, block)]
    moving_up = block
    moving_down = block
    for step in range(1, z_size // 2 + 1):
        moving_up = exchange(moving_up, "seq", ahead)
        blocks.append((step, moving_up))
        if step < z_size // 2:
            moving_down = exchange(moving_down, "seq", behind)
            blocks.append((z_size - step, moving_down))
    return [(k, mine, exchange(mine, "seq", core_pair)) for k, mine in blocks]


def place_rows(pieces, rows, tail_shape, dtype):
    seq_size = lax.axis_size("seq")
    z_size = seq_size // 4
    me = lax.axis_index("seq")
    my_z = me // 4
    my_core = me % 2
    full = jnp.zeros((z_size, 2, 2, rows) + tail_shape, dtype)
    zeros = (0,) * len(tail_shape)
    for k, mine, partner in pieces:
        z_k = (my_z - k) % z_size
        full = lax.dynamic_update_slice(full, mine[None, :, None], (z_k, 0, my_core, 0) + zeros)
        full = lax.dynamic_update_slice(
            full, partner[None, :, None], (z_k, 0, 1 - my_core, 0) + zeros
        )
    return full.reshape((z_size, 4 * rows) + tail_shape)


def tp_sum(value):
    tp_size = lax.axis_size("tp")
    total = value
    bit = 1
    while bit < tp_size:
        total = total + lax.ppermute(total, "tp", [(i, i ^ bit) for i in range(tp_size)])
        bit *= 2
    return total


def toeplitz_pair(taps):
    offsets = lax.broadcasted_iota(jnp.int32, (MR_TAPS, MR_TAPS), 0) - lax.broadcasted_iota(
        jnp.int32, (MR_TAPS, MR_TAPS), 1
    )
    lag_ids = lax.broadcasted_iota(jnp.int32, (MR_TAPS, MR_TAPS, MR_TAPS), 0)
    picks = (jnp.remainder(offsets, MR_TAPS)[None] == lag_ids).astype(jnp.bfloat16)
    table = jnp.einsum("gj,jts->gts", taps, picks, preferred_element_type=jnp.float32).astype(
        jnp.bfloat16
    )
    lower = jnp.where(offsets[None] >= 0, table, jnp.zeros_like(table))
    upper = jnp.where(offsets[None] < 0, table, jnp.zeros_like(table))
    return (lower, upper)


def project_out(y_se, w_out):
    tp_size = lax.axis_size("tp")
    stacked = lax.all_gather(w_out, "seq", axis=0, tiled=False)
    per_tp = stacked.reshape(tp_size, stacked.shape[0] // tp_size, *stacked.shape[1:])
    partial = jnp.einsum("tc,kjcf->ktjf", y_se, per_tp, preferred_element_type=jnp.float32)
    return partial.reshape(tp_size, y_se.shape[0], -1)


def per_device(qkv_se, residual, taps_se, skip_se, w_out, norm_gain, w_in, taps_mr, skip_mr):
    row_count = qkv_se.shape[0]
    chan_width = qkv_se.shape[2]
    local_groups = chan_width // GROUP
    query_se = qkv_se[:, 0].astype(jnp.float32)
    u_se = (qkv_se[:, 1].astype(jnp.float32) * qkv_se[:, 2].astype(jnp.float32)).astype(
        jnp.bfloat16
    )
    incoming_se = shifted(u_se[row_count - (SE_TAPS - 1) :], "seq", 1)
    extended = jnp.concatenate([incoming_se, u_se], axis=0).astype(jnp.float32)
    per_channel = jnp.repeat(taps_se.astype(jnp.float32), GROUP, axis=0)
    conv_se = jnp.zeros((row_count, chan_width), jnp.float32)
    for tap_index in range(SE_TAPS):
        begin = SE_TAPS - 1 - tap_index
        conv_se = conv_se + per_channel[:, tap_index] * extended[begin : begin + row_count]
    y_se = (query_se * (conv_se + skip_se.astype(jnp.float32) * u_se.astype(jnp.float32))).astype(
        jnp.bfloat16
    )
    gain_full = norm_gain.astype(jnp.float32)
    partial_out = project_out(y_se, w_out)
    share = lax.psum_scatter(partial_out, "tp", scatter_dimension=0, tiled=True)[0]
    w_full = place_rows(gather_rows(w_in), w_in.shape[0], w_in.shape[1:], w_in.dtype)
    share, w_full = lax.optimization_barrier((share, w_full))
    stream = residual.astype(jnp.float32) + share
    squares = tp_sum(jnp.sum(stream * stream, axis=1))
    scale = lax.rsqrt(squares / (chan_width * lax.axis_size("tp")) + norm_eps)
    my_gain = lax.dynamic_slice_in_dim(gain_full, lax.axis_index("tp") * chan_width, chan_width, 0)
    normed = (stream * scale[:, None] * my_gain).astype(jnp.bfloat16)
    gathered = lax.all_gather(normed, "tp", axis=0, tiled=False)
    proj = jnp.einsum("ktf,kfin->tin", gathered, w_full, preferred_element_type=jnp.float32)
    query_mr = proj[:, 0]
    u_mr = (proj[:, 1] * proj[:, 2]).astype(jnp.bfloat16)
    lower, upper = toeplitz_pair(taps_mr)
    block_count = row_count // MR_TAPS
    blocks = u_mr.reshape(block_count, MR_TAPS, local_groups, GROUP)
    inside = jnp.einsum("gts,bsgc->btgc", lower, blocks, preferred_element_type=jnp.float32)
    tail_rows = shifted(blocks[block_count - 1], "seq", 1)
    earlier = jnp.concatenate([tail_rows[None], blocks[: block_count - 1]], axis=0)
    conv_mr = inside + jnp.einsum(
        "gts,bsgc->btgc", upper, earlier, preferred_element_type=jnp.float32
    )
    conv_mr = conv_mr.reshape(row_count, chan_width)
    return (query_mr * (conv_mr + skip_mr.astype(jnp.float32) * u_mr.astype(jnp.float32))).astype(
        jnp.bfloat16
    )


def solution(mesh):
    placed = (
        P("seq", None, "tp"),
        P("seq", "tp"),
        P("tp", None),
        P("tp"),
        P("tp", "seq"),
        P(),
        P("seq", None, "tp"),
        P("tp", None),
        P("tp"),
    )
    return jax.shard_map(
        per_device, mesh=mesh, in_specs=placed, out_specs=P("seq", "tp"), check_vma=False
    )
```

```python
import jax
import jax.numpy as jnp
from jax import lax
from jax.sharding import PartitionSpec as P

GROUP = 16
SE_TAPS = 7
MR_TAPS = 128


norm_eps = 1e-05


def shifted(block, axis, distance):
    devices = range(lax.axis_size(axis))
    route = [(i - distance, i) for i in devices if i - distance in devices]
    return lax.ppermute(block, axis, route)


def seq_coords(index):
    return index // 4, (index // 2) % 2, index % 2


def seq_of(z, y_lo, core):
    return z * 4 + y_lo * 2 + core


def exchange(block, axis, pairs):
    return lax.ppermute(block, axis, pairs)


def gather_rows(piece):
    seq_size = lax.axis_size("seq")
    z_size = seq_size // 4
    me = lax.axis_index("seq")
    other = exchange(piece, "seq", [(i, i ^ 2) for i in range(seq_size)])
    mine_first = (me // 2) % 2 == 0
    block = jnp.stack(
        [jnp.where(mine_first, piece, other), jnp.where(mine_first, other, piece)]
    )
    ahead = []
    behind = []
    for i in range(seq_size):
        z, y_lo, core = seq_coords(i)
        ahead.append((i, seq_of((z + 1) % z_size, y_lo, core)))
        behind.append((i, seq_of((z - 1) % z_size, y_lo, core)))
    core_pair = [(i, i ^ 1) for i in range(seq_size)]
    blocks = [(0, block)]
    moving_up = block
    moving_down = block
    for step in range(1, z_size // 2 + 1):
        moving_up = exchange(moving_up, "seq", ahead)
        blocks.append((step, moving_up))
        if step < z_size // 2:
            moving_down = exchange(moving_down, "seq", behind)
            blocks.append((z_size - step, moving_down))
    return [(k, mine, exchange(mine, "seq", core_pair)) for k, mine in blocks]


def ring_rows(pieces):
    return jnp.stack([jnp.stack([mine, partner]) for _, mine, partner in sorted(pieces)])


def ring_features(gathered, rows):
    z_size = gathered.shape[0]
    me = lax.axis_index("seq")
    my_z = me // 4
    my_core = me % 2
    features = gathered.reshape(z_size, gathered.shape[1], 2, 2, rows)
    reverse = features[::-1]
    doubled = jnp.concatenate([reverse, reverse], axis=0)
    start = (z_size - 1 - my_z) % z_size
    by_offset = lax.dynamic_slice_in_dim(doubled, start, z_size, axis=0)
    return jnp.where(my_core == 0, by_offset, by_offset[:, :, :, ::-1])


def tp_sum(value):
    tp_size = lax.axis_size("tp")
    total = value
    bit = 1
    while bit < tp_size:
        total = total + lax.ppermute(total, "tp", [(i, i ^ bit) for i in range(tp_size)])
        bit *= 2
    return total


def toeplitz_pair(taps):
    offsets = lax.broadcasted_iota(jnp.int32, (MR_TAPS, MR_TAPS), 0) - lax.broadcasted_iota(
        jnp.int32, (MR_TAPS, MR_TAPS), 1
    )
    lag_ids = lax.broadcasted_iota(jnp.int32, (MR_TAPS, MR_TAPS, MR_TAPS), 0)
    picks = (jnp.remainder(offsets, MR_TAPS)[None] == lag_ids).astype(jnp.bfloat16)
    table = jnp.einsum("gj,jts->gts", taps, picks, preferred_element_type=jnp.float32).astype(
        jnp.bfloat16
    )
    lower = jnp.where(offsets[None] >= 0, table, jnp.zeros_like(table))
    upper = jnp.where(offsets[None] < 0, table, jnp.zeros_like(table))
    return (lower, upper)


def project_out(y_se, w_out):
    tp_size = lax.axis_size("tp")
    stacked = lax.all_gather(w_out, "seq", axis=0, tiled=False)
    per_tp = stacked.reshape(tp_size, stacked.shape[0] // tp_size, *stacked.shape[1:])
    partial = jnp.einsum("tc,kjcf->ktjf", y_se, per_tp, preferred_element_type=jnp.float32)
    return partial.reshape(tp_size, y_se.shape[0], -1)


def per_device(qkv_se, residual, taps_se, skip_se, w_out, norm_gain, w_in, taps_mr, skip_mr):
    row_count = qkv_se.shape[0]
    chan_width = qkv_se.shape[2]
    local_groups = chan_width // GROUP
    query_se = qkv_se[:, 0].astype(jnp.float32)
    u_se = (qkv_se[:, 1].astype(jnp.float32) * qkv_se[:, 2].astype(jnp.float32)).astype(
        jnp.bfloat16
    )
    incoming_se = shifted(u_se[row_count - (SE_TAPS - 1) :], "seq", 1)
    extended = jnp.concatenate([incoming_se, u_se], axis=0).astype(jnp.float32)
    per_channel = jnp.repeat(taps_se.astype(jnp.float32), GROUP, axis=0)
    conv_se = jnp.zeros((row_count, chan_width), jnp.float32)
    for tap_index in range(SE_TAPS):
        begin = SE_TAPS - 1 - tap_index
        conv_se = conv_se + per_channel[:, tap_index] * extended[begin : begin + row_count]
    y_se = (query_se * (conv_se + skip_se.astype(jnp.float32) * u_se.astype(jnp.float32))).astype(
        jnp.bfloat16
    )
    gain_full = norm_gain.astype(jnp.float32)
    partial_out = project_out(y_se, w_out)
    share = lax.psum_scatter(partial_out, "tp", scatter_dimension=0, tiled=True)[0]
    w_full = ring_rows(gather_rows(w_in))
    share, w_full = lax.optimization_barrier((share, w_full))
    stream = residual.astype(jnp.float32) + share
    squares = tp_sum(jnp.sum(stream * stream, axis=1))
    scale = lax.rsqrt(squares / (chan_width * lax.axis_size("tp")) + norm_eps)
    my_gain = lax.dynamic_slice_in_dim(gain_full, lax.axis_index("tp") * chan_width, chan_width, 0)
    normed = (stream * scale[:, None] * my_gain).astype(jnp.bfloat16)
    gathered = lax.all_gather(normed, "tp", axis=0, tiled=False)
    proj = jnp.einsum(
        "ktycr,kcyrin->tin",
        ring_features(gathered, w_in.shape[0]),
        w_full,
        preferred_element_type=jnp.float32,
    )
    query_mr = proj[:, 0]
    u_mr = (proj[:, 1] * proj[:, 2]).astype(jnp.bfloat16)
    lower, upper = toeplitz_pair(taps_mr)
    block_count = row_count // MR_TAPS
    blocks = u_mr.reshape(block_count, MR_TAPS, local_groups, GROUP)
    inside = jnp.einsum("gts,bsgc->btgc", lower, blocks, preferred_element_type=jnp.float32)
    tail_rows = shifted(blocks[block_count - 1], "seq", 1)
    earlier = jnp.concatenate([tail_rows[None], blocks[: block_count - 1]], axis=0)
    conv_mr = inside + jnp.einsum(
        "gts,bsgc->btgc", upper, earlier, preferred_element_type=jnp.float32
    )
    conv_mr = conv_mr.reshape(row_count, chan_width)
    return (query_mr * (conv_mr + skip_mr.astype(jnp.float32) * u_mr.astype(jnp.float32))).astype(
        jnp.bfloat16
    )


def solution(mesh):
    placed = (
        P("seq", None, "tp"),
        P("seq", "tp"),
        P("tp", None),
        P("tp"),
        P("tp", "seq"),
        P(),
        P("seq", None, "tp"),
        P("tp", None),
        P("tp"),
    )
    return jax.shard_map(
        per_device, mesh=mesh, in_specs=placed, out_specs=P("seq", "tp"), check_vma=False
    )
```

```python
import jax
import jax.numpy as jnp
from jax import lax
from jax.sharding import PartitionSpec as P

GROUP = 16
SE_TAPS = 7
MR_TAPS = 128


norm_eps = 1e-05


def shifted(block, axis, distance):
    devices = range(lax.axis_size(axis))
    route = [(i - distance, i) for i in devices if i - distance in devices]
    return lax.ppermute(block, axis, route)


def seq_coords(index):
    return index // 4, (index // 2) % 2, index % 2


def seq_of(z, y_lo, core):
    return z * 4 + y_lo * 2 + core


def exchange(block, axis, pairs):
    return lax.ppermute(block, axis, pairs)


def gather_rows(piece):
    seq_size = lax.axis_size("seq")
    z_size = seq_size // 4
    me = lax.axis_index("seq")
    other = exchange(piece, "seq", [(i, i ^ 2) for i in range(seq_size)])
    mine_first = (me // 2) % 2 == 0
    block = jnp.stack(
        [jnp.where(mine_first, piece, other), jnp.where(mine_first, other, piece)]
    )
    ahead = []
    behind = []
    for i in range(seq_size):
        z, y_lo, core = seq_coords(i)
        ahead.append((i, seq_of((z + 1) % z_size, y_lo, core)))
        behind.append((i, seq_of((z - 1) % z_size, y_lo, core)))
    core_pair = [(i, i ^ 1) for i in range(seq_size)]
    blocks = [(0, block)]
    moving_up = block
    moving_down = block
    for step in range(1, z_size // 2 + 1):
        moving_up = exchange(moving_up, "seq", ahead)
        blocks.append((step, moving_up))
        if step < z_size // 2:
            moving_down = exchange(moving_down, "seq", behind)
            blocks.append((z_size - step, moving_down))
    return [(k, mine, exchange(mine, "seq", core_pair)) for k, mine in blocks]


def ring_rows(pieces):
    return jnp.stack([jnp.stack([mine, partner]) for _, mine, partner in sorted(pieces)])


def ring_features(gathered, rows):
    z_size = gathered.shape[0]
    me = lax.axis_index("seq")
    my_z = me // 4
    my_core = me % 2
    features = gathered.reshape(z_size, gathered.shape[1], 2, 2, rows)
    reverse = features[::-1]
    doubled = jnp.concatenate([reverse, reverse], axis=0)
    start = (z_size - 1 - my_z) % z_size
    by_offset = lax.dynamic_slice_in_dim(doubled, start, z_size, axis=0)
    return jnp.where(my_core == 0, by_offset, by_offset[:, :, :, ::-1])


def tp_sum(value):
    tp_size = lax.axis_size("tp")
    total = value
    bit = 1
    while bit < tp_size:
        total = total + lax.ppermute(total, "tp", [(i, i ^ bit) for i in range(tp_size)])
        bit *= 2
    return total


def toeplitz_pair(taps):
    offsets = lax.broadcasted_iota(jnp.int32, (MR_TAPS, MR_TAPS), 0) - lax.broadcasted_iota(
        jnp.int32, (MR_TAPS, MR_TAPS), 1
    )
    lag_ids = lax.broadcasted_iota(jnp.int32, (MR_TAPS, MR_TAPS, MR_TAPS), 0)
    picks = (jnp.remainder(offsets, MR_TAPS)[None] == lag_ids).astype(jnp.bfloat16)
    table = jnp.einsum("gj,jts->gts", taps, picks, preferred_element_type=jnp.float32).astype(
        jnp.bfloat16
    )
    lower = jnp.where(offsets[None] >= 0, table, jnp.zeros_like(table))
    upper = jnp.where(offsets[None] < 0, table, jnp.zeros_like(table))
    return (lower, upper)


def project_out(y_se, w_out):
    tp_size = lax.axis_size("tp")
    stacked = lax.all_gather(w_out, "seq", axis=0, tiled=False)
    per_tp = stacked.reshape(tp_size, stacked.shape[0] // tp_size, *stacked.shape[1:])
    partial = jnp.einsum("tc,kjcf->ktjf", y_se, per_tp, preferred_element_type=jnp.float32)
    return partial.reshape(tp_size, y_se.shape[0], -1)


def per_device(qkv_se, residual, taps_se, skip_se, w_out, norm_gain, w_in, taps_mr, skip_mr):
    row_count = qkv_se.shape[0]
    chan_width = qkv_se.shape[2]
    local_groups = chan_width // GROUP
    query_se = qkv_se[:, 0].astype(jnp.float32)
    u_se = (qkv_se[:, 1].astype(jnp.float32) * qkv_se[:, 2].astype(jnp.float32)).astype(
        jnp.bfloat16
    )
    incoming_se = shifted(u_se[row_count - (SE_TAPS - 1) :], "seq", 1)
    extended = jnp.concatenate([incoming_se, u_se], axis=0).astype(jnp.float32)
    per_channel = jnp.repeat(taps_se.astype(jnp.float32), GROUP, axis=0)
    conv_se = jnp.zeros((row_count, chan_width), jnp.float32)
    for tap_index in range(SE_TAPS):
        begin = SE_TAPS - 1 - tap_index
        conv_se = conv_se + per_channel[:, tap_index] * extended[begin : begin + row_count]
    y_se = (query_se * (conv_se + skip_se.astype(jnp.float32) * u_se.astype(jnp.float32))).astype(
        jnp.bfloat16
    )
    gain_full = norm_gain.astype(jnp.float32)
    partial_out = project_out(y_se, w_out)
    share = lax.psum_scatter(
        partial_out.astype(jnp.bfloat16), "tp", scatter_dimension=0, tiled=True
    )[0].astype(jnp.float32)
    w_full = ring_rows(gather_rows(w_in))
    share, w_full = lax.optimization_barrier((share, w_full))
    stream = residual.astype(jnp.float32) + share
    squares = tp_sum(jnp.sum(stream * stream, axis=1))
    scale = lax.rsqrt(squares / (chan_width * lax.axis_size("tp")) + norm_eps)
    my_gain = lax.dynamic_slice_in_dim(gain_full, lax.axis_index("tp") * chan_width, chan_width, 0)
    normed = (stream * scale[:, None] * my_gain).astype(jnp.bfloat16)
    gathered = lax.all_gather(normed, "tp", axis=0, tiled=False)
    proj = jnp.einsum(
        "ktycr,kcyrin->tin",
        ring_features(gathered, w_in.shape[0]),
        w_full,
        preferred_element_type=jnp.float32,
    )
    query_mr = proj[:, 0]
    u_mr = (proj[:, 1] * proj[:, 2]).astype(jnp.bfloat16)
    lower, upper = toeplitz_pair(taps_mr)
    block_count = row_count // MR_TAPS
    blocks = u_mr.reshape(block_count, MR_TAPS, local_groups, GROUP)
    inside = jnp.einsum("gts,bsgc->btgc", lower, blocks, preferred_element_type=jnp.float32)
    tail_rows = shifted(blocks[block_count - 1], "seq", 1)
    earlier = jnp.concatenate([tail_rows[None], blocks[: block_count - 1]], axis=0)
    conv_mr = inside + jnp.einsum(
        "gts,bsgc->btgc", upper, earlier, preferred_element_type=jnp.float32
    )
    conv_mr = conv_mr.reshape(row_count, chan_width)
    return (query_mr * (conv_mr + skip_mr.astype(jnp.float32) * u_mr.astype(jnp.float32))).astype(
        jnp.bfloat16
    )


def solution(mesh):
    placed = (
        P("seq", None, "tp"),
        P("seq", "tp"),
        P("tp", None),
        P("tp"),
        P("tp", "seq"),
        P(),
        P("seq", None, "tp"),
        P("tp", None),
        P("tp"),
    )
    return jax.shard_map(
        per_device, mesh=mesh, in_specs=placed, out_specs=P("seq", "tp"), check_vma=False
    )
```

```python
import jax
import jax.numpy as jnp
from jax import lax
from jax.sharding import PartitionSpec as P

GROUP = 16
SE_TAPS = 7
MR_TAPS = 128


norm_eps = 1e-05


def shifted(block, axis, distance):
    devices = range(lax.axis_size(axis))
    route = [(i - distance, i) for i in devices if i - distance in devices]
    return lax.ppermute(block, axis, route)


def seq_coords(index):
    return index // 4, (index // 2) % 2, index % 2


def seq_of(z, y_lo, core):
    return z * 4 + y_lo * 2 + core


def exchange(block, axis, pairs):
    return lax.ppermute(block, axis, pairs)


def gather_rows(piece):
    seq_size = lax.axis_size("seq")
    z_size = seq_size // 4
    me = lax.axis_index("seq")
    other = exchange(piece, "seq", [(i, i ^ 2) for i in range(seq_size)])
    mine_first = (me // 2) % 2 == 0
    block = jnp.stack(
        [jnp.where(mine_first, piece, other), jnp.where(mine_first, other, piece)]
    )
    ahead = []
    behind = []
    for i in range(seq_size):
        z, y_lo, core = seq_coords(i)
        ahead.append((i, seq_of((z + 1) % z_size, y_lo, core)))
        behind.append((i, seq_of((z - 1) % z_size, y_lo, core)))
    core_pair = [(i, i ^ 1) for i in range(seq_size)]
    blocks = [(0, block)]
    moving_up = block
    moving_down = block
    for step in range(1, z_size // 2 + 1):
        moving_up = exchange(moving_up, "seq", ahead)
        blocks.append((step, moving_up))
        if step < z_size // 2:
            moving_down = exchange(moving_down, "seq", behind)
            blocks.append((z_size - step, moving_down))
    return [(k, mine, exchange(mine, "seq", core_pair)) for k, mine in blocks]


def absolute_rows(pieces):
    me = lax.axis_index("seq")
    my_z = me // 4
    mine_first = me % 2 == 0
    by_offset = jnp.stack(
        [
            jnp.where(
                mine_first, jnp.stack([mine, partner], axis=1), jnp.stack([partner, mine], axis=1)
            )
            for _, mine, partner in sorted(pieces)
        ]
    )
    z_size = by_offset.shape[0]
    reverse = by_offset[::-1]
    doubled = jnp.concatenate([reverse, reverse], axis=0)
    return lax.dynamic_slice_in_dim(doubled, (z_size - 1 - my_z) % z_size, z_size, axis=0)


def tp_sum(value):
    tp_size = lax.axis_size("tp")
    total = value
    bit = 1
    while bit < tp_size:
        total = total + lax.ppermute(total, "tp", [(i, i ^ bit) for i in range(tp_size)])
        bit *= 2
    return total


def toeplitz_pair(taps):
    offsets = lax.broadcasted_iota(jnp.int32, (MR_TAPS, MR_TAPS), 0) - lax.broadcasted_iota(
        jnp.int32, (MR_TAPS, MR_TAPS), 1
    )
    lag_ids = lax.broadcasted_iota(jnp.int32, (MR_TAPS, MR_TAPS, MR_TAPS), 0)
    picks = (jnp.remainder(offsets, MR_TAPS)[None] == lag_ids).astype(jnp.bfloat16)
    table = jnp.einsum("gj,jts->gts", taps, picks, preferred_element_type=jnp.float32).astype(
        jnp.bfloat16
    )
    lower = jnp.where(offsets[None] >= 0, table, jnp.zeros_like(table))
    upper = jnp.where(offsets[None] < 0, table, jnp.zeros_like(table))
    return (lower, upper)


def project_out(y_se, w_out):
    tp_size = lax.axis_size("tp")
    stacked = lax.all_gather(w_out, "seq", axis=0, tiled=False)
    per_tp = stacked.reshape(tp_size, stacked.shape[0] // tp_size, *stacked.shape[1:])
    partial = jnp.einsum("tc,kjcf->ktjf", y_se, per_tp, preferred_element_type=jnp.float32)
    return partial.reshape(tp_size, y_se.shape[0], -1)


def per_device(qkv_se, residual, taps_se, skip_se, w_out, norm_gain, w_in, taps_mr, skip_mr):
    row_count = qkv_se.shape[0]
    chan_width = qkv_se.shape[2]
    local_groups = chan_width // GROUP
    query_se = qkv_se[:, 0].astype(jnp.float32)
    u_se = (qkv_se[:, 1].astype(jnp.float32) * qkv_se[:, 2].astype(jnp.float32)).astype(
        jnp.bfloat16
    )
    incoming_se = shifted(u_se[row_count - (SE_TAPS - 1) :], "seq", 1)
    extended = jnp.concatenate([incoming_se, u_se], axis=0).astype(jnp.float32)
    per_channel = jnp.repeat(taps_se.astype(jnp.float32), GROUP, axis=0)
    conv_se = jnp.zeros((row_count, chan_width), jnp.float32)
    for tap_index in range(SE_TAPS):
        begin = SE_TAPS - 1 - tap_index
        conv_se = conv_se + per_channel[:, tap_index] * extended[begin : begin + row_count]
    y_se = (query_se * (conv_se + skip_se.astype(jnp.float32) * u_se.astype(jnp.float32))).astype(
        jnp.bfloat16
    )
    gain_full = norm_gain.astype(jnp.float32)
    partial_out = project_out(y_se, w_out)
    share = lax.psum_scatter(partial_out, "tp", scatter_dimension=0, tiled=True)[0]
    w_full = absolute_rows(gather_rows(w_in))
    share, w_full = lax.optimization_barrier((share, w_full))
    stream = residual.astype(jnp.float32) + share
    squares = tp_sum(jnp.sum(stream * stream, axis=1))
    scale = lax.rsqrt(squares / (chan_width * lax.axis_size("tp")) + norm_eps)
    my_gain = lax.dynamic_slice_in_dim(gain_full, lax.axis_index("tp") * chan_width, chan_width, 0)
    normed = (stream * scale[:, None] * my_gain).astype(jnp.bfloat16)
    gathered = lax.all_gather(normed, "tp", axis=0, tiled=False)
    proj = jnp.einsum(
        "ktf,kfin->tin",
        gathered,
        w_full.reshape(gathered.shape[0], gathered.shape[2], *w_in.shape[1:]),
        preferred_element_type=jnp.float32,
    )
    query_mr = proj[:, 0]
    u_mr = (proj[:, 1] * proj[:, 2]).astype(jnp.bfloat16)
    lower, upper = toeplitz_pair(taps_mr)
    block_count = row_count // MR_TAPS
    blocks = u_mr.reshape(block_count, MR_TAPS, local_groups, GROUP)
    inside = jnp.einsum("gts,bsgc->btgc", lower, blocks, preferred_element_type=jnp.float32)
    tail_rows = shifted(blocks[block_count - 1], "seq", 1)
    earlier = jnp.concatenate([tail_rows[None], blocks[: block_count - 1]], axis=0)
    conv_mr = inside + jnp.einsum(
        "gts,bsgc->btgc", upper, earlier, preferred_element_type=jnp.float32
    )
    conv_mr = conv_mr.reshape(row_count, chan_width)
    return (query_mr * (conv_mr + skip_mr.astype(jnp.float32) * u_mr.astype(jnp.float32))).astype(
        jnp.bfloat16
    )


def solution(mesh):
    placed = (
        P("seq", None, "tp"),
        P("seq", "tp"),
        P("tp", None),
        P("tp"),
        P("tp", "seq"),
        P(),
        P("seq", None, "tp"),
        P("tp", None),
        P("tp"),
    )
    return jax.shard_map(
        per_device, mesh=mesh, in_specs=placed, out_specs=P("seq", "tp"), check_vma=False
    )
```

```python
import jax
import jax.numpy as jnp
from jax import lax
from jax.sharding import PartitionSpec as P

GROUP = 16
SE_TAPS = 7
MR_TAPS = 128


norm_eps = 1e-05


def shifted(block, axis, distance):
    devices = range(lax.axis_size(axis))
    route = [(i - distance, i) for i in devices if i - distance in devices]
    return lax.ppermute(block, axis, route)


def seq_coords(index):
    return index // 4, (index // 2) % 2, index % 2


def seq_of(z, y_lo, core):
    return z * 4 + y_lo * 2 + core


def exchange(block, axis, pairs):
    return lax.ppermute(block, axis, pairs)


def gather_rows(piece):
    seq_size = lax.axis_size("seq")
    z_size = seq_size // 4
    me = lax.axis_index("seq")
    other = exchange(piece, "seq", [(i, i ^ 2) for i in range(seq_size)])
    mine_first = (me // 2) % 2 == 0
    block = jnp.stack(
        [jnp.where(mine_first, piece, other), jnp.where(mine_first, other, piece)]
    )
    ahead = []
    behind = []
    for i in range(seq_size):
        z, y_lo, core = seq_coords(i)
        ahead.append((i, seq_of((z + 1) % z_size, y_lo, core)))
        behind.append((i, seq_of((z - 1) % z_size, y_lo, core)))
    core_pair = [(i, i ^ 1) for i in range(seq_size)]
    blocks = [(0, block)]
    moving_up = block
    moving_down = block
    for step in range(1, z_size // 2 + 1):
        moving_up = exchange(moving_up, "seq", ahead)
        blocks.append((step, moving_up))
        if step < z_size // 2:
            moving_down = exchange(moving_down, "seq", behind)
            blocks.append((z_size - step, moving_down))
    return [(k, mine, exchange(mine, "seq", core_pair)) for k, mine in blocks]


def absolute_rows(pieces):
    me = lax.axis_index("seq")
    my_z = me // 4
    mine_first = me % 2 == 0
    z_size = len(pieces)
    full = None
    for k, mine, partner in sorted(pieces):
        block = jnp.where(
            mine_first, jnp.stack([mine, partner], axis=1), jnp.stack([partner, mine], axis=1)
        )
        if full is None:
            full = jnp.zeros((z_size,) + block.shape, block.dtype)
        start = ((my_z - k) % z_size,) + (0,) * block.ndim
        full = lax.dynamic_update_slice(full, block[None], start)
    return full


def tp_sum(value):
    tp_size = lax.axis_size("tp")
    total = value
    bit = 1
    while bit < tp_size:
        total = total + lax.ppermute(total, "tp", [(i, i ^ bit) for i in range(tp_size)])
        bit *= 2
    return total


def toeplitz_pair(taps):
    offsets = lax.broadcasted_iota(jnp.int32, (MR_TAPS, MR_TAPS), 0) - lax.broadcasted_iota(
        jnp.int32, (MR_TAPS, MR_TAPS), 1
    )
    lag_ids = lax.broadcasted_iota(jnp.int32, (MR_TAPS, MR_TAPS, MR_TAPS), 0)
    picks = (jnp.remainder(offsets, MR_TAPS)[None] == lag_ids).astype(jnp.bfloat16)
    table = jnp.einsum("gj,jts->gts", taps, picks, preferred_element_type=jnp.float32).astype(
        jnp.bfloat16
    )
    lower = jnp.where(offsets[None] >= 0, table, jnp.zeros_like(table))
    upper = jnp.where(offsets[None] < 0, table, jnp.zeros_like(table))
    return (lower, upper)


def project_out(y_se, w_out):
    tp_size = lax.axis_size("tp")
    stacked = lax.all_gather(w_out, "seq", axis=0, tiled=False)
    per_tp = stacked.reshape(tp_size, stacked.shape[0] // tp_size, *stacked.shape[1:])
    partial = jnp.einsum("tc,kjcf->tkjf", y_se, per_tp, preferred_element_type=jnp.float32)
    return partial.reshape(y_se.shape[0], tp_size, -1)


def per_device(qkv_se, residual, taps_se, skip_se, w_out, norm_gain, w_in, taps_mr, skip_mr):
    row_count = qkv_se.shape[0]
    chan_width = qkv_se.shape[2]
    local_groups = chan_width // GROUP
    query_se = qkv_se[:, 0].astype(jnp.float32)
    u_se = (qkv_se[:, 1].astype(jnp.float32) * qkv_se[:, 2].astype(jnp.float32)).astype(
        jnp.bfloat16
    )
    incoming_se = shifted(u_se[row_count - (SE_TAPS - 1) :], "seq", 1)
    extended = jnp.concatenate([incoming_se, u_se], axis=0).astype(jnp.float32)
    per_channel = jnp.repeat(taps_se.astype(jnp.float32), GROUP, axis=0)
    conv_se = jnp.zeros((row_count, chan_width), jnp.float32)
    for tap_index in range(SE_TAPS):
        begin = SE_TAPS - 1 - tap_index
        conv_se = conv_se + per_channel[:, tap_index] * extended[begin : begin + row_count]
    y_se = (query_se * (conv_se + skip_se.astype(jnp.float32) * u_se.astype(jnp.float32))).astype(
        jnp.bfloat16
    )
    gain_full = norm_gain.astype(jnp.float32)
    partial_out = project_out(y_se, w_out)
    share = lax.psum_scatter(partial_out, "tp", scatter_dimension=1, tiled=True)[:, 0]
    w_full = absolute_rows(gather_rows(w_in))
    share, w_full = lax.optimization_barrier((share, w_full))
    stream = residual.astype(jnp.float32) + share
    squares = tp_sum(jnp.sum(stream * stream, axis=1))
    scale = lax.rsqrt(squares / (chan_width * lax.axis_size("tp")) + norm_eps)
    my_gain = lax.dynamic_slice_in_dim(gain_full, lax.axis_index("tp") * chan_width, chan_width, 0)
    normed = (stream * scale[:, None] * my_gain).astype(jnp.bfloat16)
    gathered = lax.all_gather(normed, "tp", axis=0, tiled=False)
    proj = jnp.einsum(
        "ktf,kfin->tin",
        gathered,
        w_full.reshape(gathered.shape[0], gathered.shape[2], *w_in.shape[1:]),
        preferred_element_type=jnp.float32,
    )
    query_mr = proj[:, 0]
    u_mr = (proj[:, 1] * proj[:, 2]).astype(jnp.bfloat16)
    lower, upper = toeplitz_pair(taps_mr)
    block_count = row_count // MR_TAPS
    blocks = u_mr.reshape(block_count, MR_TAPS, local_groups, GROUP)
    inside = jnp.einsum("gts,bsgc->btgc", lower, blocks, preferred_element_type=jnp.float32)
    tail_rows = shifted(blocks[block_count - 1], "seq", 1)
    earlier = jnp.concatenate([tail_rows[None], blocks[: block_count - 1]], axis=0)
    conv_mr = inside + jnp.einsum(
        "gts,bsgc->btgc", upper, earlier, preferred_element_type=jnp.float32
    )
    conv_mr = conv_mr.reshape(row_count, chan_width)
    return (query_mr * (conv_mr + skip_mr.astype(jnp.float32) * u_mr.astype(jnp.float32))).astype(
        jnp.bfloat16
    )


def solution(mesh):
    placed = (
        P("seq", None, "tp"),
        P("seq", "tp"),
        P("tp", None),
        P("tp"),
        P("tp", "seq"),
        P(),
        P("seq", None, "tp"),
        P("tp", None),
        P("tp"),
    )
    return jax.shard_map(
        per_device, mesh=mesh, in_specs=placed, out_specs=P("seq", "tp"), check_vma=False
    )
```

```python
import jax
import jax.numpy as jnp
from jax import lax
from jax.sharding import PartitionSpec as P

GROUP = 16
SE_TAPS = 7
MR_TAPS = 128


norm_eps = 1e-05


def shifted(block, axis, distance):
    devices = range(lax.axis_size(axis))
    route = [(i - distance, i) for i in devices if i - distance in devices]
    return lax.ppermute(block, axis, route)


def seq_coords(index):
    return index // 4, (index // 2) % 2, index % 2


def seq_of(z, y_lo, core):
    return z * 4 + y_lo * 2 + core


def exchange(block, axis, pairs):
    return lax.ppermute(block, axis, pairs)


def gather_rows(piece):
    seq_size = lax.axis_size("seq")
    z_size = seq_size // 4
    me = lax.axis_index("seq")
    other = exchange(piece, "seq", [(i, i ^ 2) for i in range(seq_size)])
    mine_first = (me // 2) % 2 == 0
    block = jnp.stack(
        [jnp.where(mine_first, piece, other), jnp.where(mine_first, other, piece)]
    )
    ahead = []
    behind = []
    for i in range(seq_size):
        z, y_lo, core = seq_coords(i)
        ahead.append((i, seq_of((z + 1) % z_size, y_lo, core)))
        behind.append((i, seq_of((z - 1) % z_size, y_lo, core)))
    core_pair = [(i, i ^ 1) for i in range(seq_size)]
    blocks = [(0, block)]
    moving_up = block
    moving_down = block
    for step in range(1, z_size // 2 + 1):
        moving_up = exchange(moving_up, "seq", ahead)
        blocks.append((step, moving_up))
        if step < z_size // 2:
            moving_down = exchange(moving_down, "seq", behind)
            blocks.append((z_size - step, moving_down))
    return [(k, mine, exchange(mine, "seq", core_pair)) for k, mine in blocks]


def absolute_rows(pieces):
    me = lax.axis_index("seq")
    my_z = me // 4
    mine_first = me % 2 == 0
    by_offset = jnp.stack(
        [
            jnp.where(
                mine_first, jnp.stack([mine, partner], axis=1), jnp.stack([partner, mine], axis=1)
            )
            for _, mine, partner in sorted(pieces)
        ]
    )
    z_size = by_offset.shape[0]
    reverse = by_offset[::-1]
    doubled = jnp.concatenate([reverse, reverse], axis=0)
    return lax.dynamic_slice_in_dim(doubled, (z_size - 1 - my_z) % z_size, z_size, axis=0)


def tp_sum(value):
    tp_size = lax.axis_size("tp")
    total = value
    bit = 1
    while bit < tp_size:
        total = total + lax.ppermute(total, "tp", [(i, i ^ bit) for i in range(tp_size)])
        bit *= 2
    return total


def toeplitz_pair(taps):
    offsets = lax.broadcasted_iota(jnp.int32, (MR_TAPS, MR_TAPS), 0) - lax.broadcasted_iota(
        jnp.int32, (MR_TAPS, MR_TAPS), 1
    )
    lag_ids = lax.broadcasted_iota(jnp.int32, (MR_TAPS, MR_TAPS, MR_TAPS), 0)
    picks = (jnp.remainder(offsets, MR_TAPS)[None] == lag_ids).astype(jnp.bfloat16)
    table = jnp.einsum("gj,jts->gts", taps, picks, preferred_element_type=jnp.float32).astype(
        jnp.bfloat16
    )
    lower = jnp.where(offsets[None] >= 0, table, jnp.zeros_like(table))
    upper = jnp.where(offsets[None] < 0, table, jnp.zeros_like(table))
    return (lower, upper)


def project_out(y_se, w_out):
    by_z = absolute_rows(gather_rows(w_out))
    partial = jnp.einsum("tc,zyxcf->tzyxf", y_se, by_z, preferred_element_type=jnp.float32)
    return partial.reshape(y_se.shape[0], by_z.shape[0], -1)


def per_device(qkv_se, residual, taps_se, skip_se, w_out, norm_gain, w_in, taps_mr, skip_mr):
    row_count = qkv_se.shape[0]
    chan_width = qkv_se.shape[2]
    local_groups = chan_width // GROUP
    query_se = qkv_se[:, 0].astype(jnp.float32)
    u_se = (qkv_se[:, 1].astype(jnp.float32) * qkv_se[:, 2].astype(jnp.float32)).astype(
        jnp.bfloat16
    )
    incoming_se = shifted(u_se[row_count - (SE_TAPS - 1) :], "seq", 1)
    extended = jnp.concatenate([incoming_se, u_se], axis=0).astype(jnp.float32)
    per_channel = jnp.repeat(taps_se.astype(jnp.float32), GROUP, axis=0)
    conv_se = jnp.zeros((row_count, chan_width), jnp.float32)
    for tap_index in range(SE_TAPS):
        begin = SE_TAPS - 1 - tap_index
        conv_se = conv_se + per_channel[:, tap_index] * extended[begin : begin + row_count]
    y_se = (query_se * (conv_se + skip_se.astype(jnp.float32) * u_se.astype(jnp.float32))).astype(
        jnp.bfloat16
    )
    gain_full = norm_gain.astype(jnp.float32)
    partial_out = project_out(y_se, w_out)
    share = lax.psum_scatter(partial_out, "tp", scatter_dimension=1, tiled=True)[:, 0]
    w_in_after, _ = lax.optimization_barrier((w_in, partial_out))
    w_full = absolute_rows(gather_rows(w_in_after))
    share, w_full = lax.optimization_barrier((share, w_full))
    stream = residual.astype(jnp.float32) + share
    squares = tp_sum(jnp.sum(stream * stream, axis=1))
    scale = lax.rsqrt(squares / (chan_width * lax.axis_size("tp")) + norm_eps)
    my_gain = lax.dynamic_slice_in_dim(gain_full, lax.axis_index("tp") * chan_width, chan_width, 0)
    normed = (stream * scale[:, None] * my_gain).astype(jnp.bfloat16)
    gathered = lax.all_gather(normed, "tp", axis=0, tiled=False)
    proj = jnp.einsum(
        "ktf,kfin->tin",
        gathered,
        w_full.reshape(gathered.shape[0], gathered.shape[2], *w_in.shape[1:]),
        preferred_element_type=jnp.float32,
    )
    query_mr = proj[:, 0]
    u_mr = (proj[:, 1] * proj[:, 2]).astype(jnp.bfloat16)
    lower, upper = toeplitz_pair(taps_mr)
    block_count = row_count // MR_TAPS
    blocks = u_mr.reshape(block_count, MR_TAPS, local_groups, GROUP)
    inside = jnp.einsum("gts,bsgc->btgc", lower, blocks, preferred_element_type=jnp.float32)
    tail_rows = shifted(blocks[block_count - 1], "seq", 1)
    earlier = jnp.concatenate([tail_rows[None], blocks[: block_count - 1]], axis=0)
    conv_mr = inside + jnp.einsum(
        "gts,bsgc->btgc", upper, earlier, preferred_element_type=jnp.float32
    )
    conv_mr = conv_mr.reshape(row_count, chan_width)
    return (query_mr * (conv_mr + skip_mr.astype(jnp.float32) * u_mr.astype(jnp.float32))).astype(
        jnp.bfloat16
    )


def solution(mesh):
    placed = (
        P("seq", None, "tp"),
        P("seq", "tp"),
        P("tp", None),
        P("tp"),
        P("tp", "seq"),
        P(),
        P("seq", None, "tp"),
        P("tp", None),
        P("tp"),
    )
    return jax.shard_map(
        per_device, mesh=mesh, in_specs=placed, out_specs=P("seq", "tp"), check_vma=False
    )
```

```python
import jax
import jax.numpy as jnp
from jax import lax
from jax.sharding import PartitionSpec as P

GROUP = 16
SE_TAPS = 7
MR_TAPS = 128


norm_eps = 1e-05


def shifted(block, axis, distance):
    devices = range(lax.axis_size(axis))
    route = [(i - distance, i) for i in devices if i - distance in devices]
    return lax.ppermute(block, axis, route)


def seq_coords(index):
    return index // 4, (index // 2) % 2, index % 2


def seq_of(z, y_lo, core):
    return z * 4 + y_lo * 2 + core


def exchange(block, axis, pairs):
    return lax.ppermute(block, axis, pairs)


def gather_rows(piece):
    seq_size = lax.axis_size("seq")
    z_size = seq_size // 4
    me = lax.axis_index("seq")
    other = exchange(piece, "seq", [(i, i ^ 2) for i in range(seq_size)])
    mine_first = (me // 2) % 2 == 0
    block = jnp.stack(
        [jnp.where(mine_first, piece, other), jnp.where(mine_first, other, piece)]
    )
    ahead = []
    behind = []
    for i in range(seq_size):
        z, y_lo, core = seq_coords(i)
        ahead.append((i, seq_of((z + 1) % z_size, y_lo, core)))
        behind.append((i, seq_of((z - 1) % z_size, y_lo, core)))
    core_pair = [(i, i ^ 1) for i in range(seq_size)]
    blocks = [(0, block)]
    moving_up = block
    moving_down = block
    for step in range(1, z_size // 2 + 1):
        moving_up = exchange(moving_up, "seq", ahead)
        blocks.append((step, moving_up))
        if step < z_size // 2:
            moving_down = exchange(moving_down, "seq", behind)
            blocks.append((z_size - step, moving_down))
    return [(k, mine, exchange(mine, "seq", core_pair)) for k, mine in blocks]


def absolute_rows(pieces):
    me = lax.axis_index("seq")
    my_z = me // 4
    mine_first = me % 2 == 0
    by_offset = jnp.stack(
        [
            jnp.where(
                mine_first, jnp.stack([mine, partner], axis=1), jnp.stack([partner, mine], axis=1)
            )
            for _, mine, partner in sorted(pieces)
        ]
    )
    z_size = by_offset.shape[0]
    reverse = by_offset[::-1]
    doubled = jnp.concatenate([reverse, reverse], axis=0)
    return lax.dynamic_slice_in_dim(doubled, (z_size - 1 - my_z) % z_size, z_size, axis=0)


def tp_sum(value):
    tp_size = lax.axis_size("tp")
    total = value
    for offset in range(1, tp_size):
        total = total + lax.ppermute(
            value, "tp", [(i, (i + offset) % tp_size) for i in range(tp_size)]
        )
    return total


def tp_gather(block):
    tp_size = lax.axis_size("tp")
    x_size = tp_size // 2
    me = lax.axis_index("tp")
    my_x = me % x_size
    y_first = me // x_size == 0
    other = lax.ppermute(block, "tp", [(i, i ^ x_size) for i in range(tp_size)])
    pair = jnp.stack([jnp.where(y_first, block, other), jnp.where(y_first, other, block)])
    up = [(i, (i // x_size) * x_size + (i % x_size + 1) % x_size) for i in range(tp_size)]
    down = [(i, (i // x_size) * x_size + (i % x_size - 1) % x_size) for i in range(tp_size)]
    from_below = lax.ppermute(pair, "tp", up)
    from_above = lax.ppermute(pair, "tp", down)
    from_far = lax.ppermute(from_below, "tp", up)
    by_offset = jnp.stack([pair, from_above, from_far, from_below])
    doubled = jnp.concatenate([by_offset, by_offset], axis=0)
    by_x = lax.dynamic_slice_in_dim(doubled, (x_size - my_x) % x_size, x_size, axis=0)
    return jnp.swapaxes(by_x, 0, 1).reshape(tp_size, *block.shape)


def toeplitz_pair(taps):
    offsets = lax.broadcasted_iota(jnp.int32, (MR_TAPS, MR_TAPS), 0) - lax.broadcasted_iota(
        jnp.int32, (MR_TAPS, MR_TAPS), 1
    )
    lag_ids = lax.broadcasted_iota(jnp.int32, (MR_TAPS, MR_TAPS, MR_TAPS), 0)
    picks = (jnp.remainder(offsets, MR_TAPS)[None] == lag_ids).astype(jnp.bfloat16)
    table = jnp.einsum("gj,jts->gts", taps, picks, preferred_element_type=jnp.float32).astype(
        jnp.bfloat16
    )
    lower = jnp.where(offsets[None] >= 0, table, jnp.zeros_like(table))
    upper = jnp.where(offsets[None] < 0, table, jnp.zeros_like(table))
    return (lower, upper)


def project_out(y_se, w_out):
    by_z = absolute_rows(gather_rows(w_out))
    partial = jnp.einsum("tc,zyxcf->tzyxf", y_se, by_z, preferred_element_type=jnp.float32)
    return partial.reshape(y_se.shape[0], by_z.shape[0], -1)


def per_device(qkv_se, residual, taps_se, skip_se, w_out, norm_gain, w_in, taps_mr, skip_mr):
    row_count = qkv_se.shape[0]
    chan_width = qkv_se.shape[2]
    local_groups = chan_width // GROUP
    query_se = qkv_se[:, 0].astype(jnp.float32)
    u_se = (qkv_se[:, 1].astype(jnp.float32) * qkv_se[:, 2].astype(jnp.float32)).astype(
        jnp.bfloat16
    )
    incoming_se = shifted(u_se[row_count - (SE_TAPS - 1) :], "seq", 1)
    extended = jnp.concatenate([incoming_se, u_se], axis=0).astype(jnp.float32)
    per_channel = jnp.repeat(taps_se.astype(jnp.float32), GROUP, axis=0)
    conv_se = jnp.zeros((row_count, chan_width), jnp.float32)
    for tap_index in range(SE_TAPS):
        begin = SE_TAPS - 1 - tap_index
        conv_se = conv_se + per_channel[:, tap_index] * extended[begin : begin + row_count]
    y_se = (query_se * (conv_se + skip_se.astype(jnp.float32) * u_se.astype(jnp.float32))).astype(
        jnp.bfloat16
    )
    gain_full = norm_gain.astype(jnp.float32)
    partial_out = project_out(y_se, w_out)
    share = lax.psum_scatter(partial_out, "tp", scatter_dimension=1, tiled=True)[:, 0]
    w_in_after, _ = lax.optimization_barrier((w_in, partial_out))
    w_full = absolute_rows(gather_rows(w_in_after))
    share, w_full = lax.optimization_barrier((share, w_full))
    stream = residual.astype(jnp.float32) + share
    squares = tp_sum(jnp.sum(stream * stream, axis=1))
    scale = lax.rsqrt(squares / (chan_width * lax.axis_size("tp")) + norm_eps)
    my_gain = lax.dynamic_slice_in_dim(gain_full, lax.axis_index("tp") * chan_width, chan_width, 0)
    normed = (stream * scale[:, None] * my_gain).astype(jnp.bfloat16)
    half = row_count // 2
    gathered_sc = lax.all_gather(normed[:half], "tp", axis=0, tiled=False)
    gathered_ring = tp_gather(normed[half:])
    weights = w_full.reshape(gathered_sc.shape[0], gathered_sc.shape[2], *w_in.shape[1:])
    proj = jnp.concatenate(
        [
            jnp.einsum("ktf,kfin->tin", part, weights, preferred_element_type=jnp.float32)
            for part in (gathered_sc, gathered_ring)
        ],
        axis=0,
    )
    query_mr = proj[:, 0]
    u_mr = (proj[:, 1] * proj[:, 2]).astype(jnp.bfloat16)
    lower, upper = toeplitz_pair(taps_mr)
    block_count = row_count // MR_TAPS
    blocks = u_mr.reshape(block_count, MR_TAPS, local_groups, GROUP)
    inside = jnp.einsum("gts,bsgc->btgc", lower, blocks, preferred_element_type=jnp.float32)
    tail_rows = shifted(blocks[block_count - 1], "seq", 1)
    earlier = jnp.concatenate([tail_rows[None], blocks[: block_count - 1]], axis=0)
    conv_mr = inside + jnp.einsum(
        "gts,bsgc->btgc", upper, earlier, preferred_element_type=jnp.float32
    )
    conv_mr = conv_mr.reshape(row_count, chan_width)
    return (query_mr * (conv_mr + skip_mr.astype(jnp.float32) * u_mr.astype(jnp.float32))).astype(
        jnp.bfloat16
    )


def solution(mesh):
    placed = (
        P("seq", None, "tp"),
        P("seq", "tp"),
        P("tp", None),
        P("tp"),
        P("tp", "seq"),
        P(),
        P("seq", None, "tp"),
        P("tp", None),
        P("tp"),
    )
    return jax.shard_map(
        per_device, mesh=mesh, in_specs=placed, out_specs=P("seq", "tp"), check_vma=False
    )
```

```python
import jax
import jax.numpy as jnp
from jax import lax
from jax.sharding import PartitionSpec as P

GROUP = 16
SE_TAPS = 7
MR_TAPS = 128


norm_eps = 1e-05


def shifted(block, axis, distance):
    devices = range(lax.axis_size(axis))
    route = [(i - distance, i) for i in devices if i - distance in devices]
    return lax.ppermute(block, axis, route)


def seq_coords(index):
    return index // 4, (index // 2) % 2, index % 2


def seq_of(z, y_lo, core):
    return z * 4 + y_lo * 2 + core


def exchange(block, axis, pairs):
    return lax.ppermute(block, axis, pairs)


def gather_rows(piece):
    seq_size = lax.axis_size("seq")
    z_size = seq_size // 4
    me = lax.axis_index("seq")
    other = exchange(piece, "seq", [(i, i ^ 2) for i in range(seq_size)])
    mine_first = (me // 2) % 2 == 0
    block = jnp.stack(
        [jnp.where(mine_first, piece, other), jnp.where(mine_first, other, piece)]
    )
    ahead = []
    behind = []
    for i in range(seq_size):
        z, y_lo, core = seq_coords(i)
        ahead.append((i, seq_of((z + 1) % z_size, y_lo, core)))
        behind.append((i, seq_of((z - 1) % z_size, y_lo, core)))
    core_pair = [(i, i ^ 1) for i in range(seq_size)]
    blocks = [(0, block)]
    moving_up = block
    moving_down = block
    for step in range(1, z_size // 2 + 1):
        moving_up = exchange(moving_up, "seq", ahead)
        blocks.append((step, moving_up))
        if step < z_size // 2:
            moving_down = exchange(moving_down, "seq", behind)
            blocks.append((z_size - step, moving_down))
    return [(k, mine, exchange(mine, "seq", core_pair)) for k, mine in blocks]


def absolute_rows(pieces):
    me = lax.axis_index("seq")
    my_z = me // 4
    mine_first = me % 2 == 0
    by_offset = jnp.stack(
        [
            jnp.where(
                mine_first, jnp.stack([mine, partner], axis=1), jnp.stack([partner, mine], axis=1)
            )
            for _, mine, partner in sorted(pieces)
        ]
    )
    z_size = by_offset.shape[0]
    reverse = by_offset[::-1]
    doubled = jnp.concatenate([reverse, reverse], axis=0)
    return lax.dynamic_slice_in_dim(doubled, (z_size - 1 - my_z) % z_size, z_size, axis=0)


def tp_sum(value):
    tp_size = lax.axis_size("tp")
    total = value
    for offset in range(1, tp_size):
        total = total + lax.ppermute(
            value, "tp", [(i, (i + offset) % tp_size) for i in range(tp_size)]
        )
    return total


def tp_gather(block):
    tp_size = lax.axis_size("tp")
    x_size = tp_size // 2
    me = lax.axis_index("tp")
    my_x = me % x_size
    y_first = me // x_size == 0
    other = lax.ppermute(block, "tp", [(i, i ^ x_size) for i in range(tp_size)])
    pair = jnp.stack([jnp.where(y_first, block, other), jnp.where(y_first, other, block)])
    up = [(i, (i // x_size) * x_size + (i % x_size + 1) % x_size) for i in range(tp_size)]
    down = [(i, (i // x_size) * x_size + (i % x_size - 1) % x_size) for i in range(tp_size)]
    from_below = lax.ppermute(pair, "tp", up)
    from_above = lax.ppermute(pair, "tp", down)
    from_far = lax.ppermute(from_below, "tp", up)
    by_offset = jnp.stack([pair, from_above, from_far, from_below])
    doubled = jnp.concatenate([by_offset, by_offset], axis=0)
    by_x = lax.dynamic_slice_in_dim(doubled, (x_size - my_x) % x_size, x_size, axis=0)
    return jnp.swapaxes(by_x, 0, 1).reshape(tp_size, *block.shape)


def toeplitz_pair(taps):
    offsets = lax.broadcasted_iota(jnp.int32, (MR_TAPS, MR_TAPS), 0) - lax.broadcasted_iota(
        jnp.int32, (MR_TAPS, MR_TAPS), 1
    )
    lag_ids = lax.broadcasted_iota(jnp.int32, (MR_TAPS, MR_TAPS, MR_TAPS), 0)
    picks = (jnp.remainder(offsets, MR_TAPS)[None] == lag_ids).astype(jnp.bfloat16)
    table = jnp.einsum("gj,jts->gts", taps, picks, preferred_element_type=jnp.float32).astype(
        jnp.bfloat16
    )
    lower = jnp.where(offsets[None] >= 0, table, jnp.zeros_like(table))
    upper = jnp.where(offsets[None] < 0, table, jnp.zeros_like(table))
    return (lower, upper)


def project_out(y_se, w_out):
    by_z = absolute_rows(gather_rows(w_out))
    partial = jnp.einsum("tc,zyxcf->tzyxf", y_se, by_z, preferred_element_type=jnp.float32)
    return partial.reshape(y_se.shape[0], by_z.shape[0], -1)


def per_device(qkv_se, residual, taps_se, skip_se, w_out, norm_gain, w_in, taps_mr, skip_mr):
    row_count = qkv_se.shape[0]
    chan_width = qkv_se.shape[2]
    local_groups = chan_width // GROUP
    query_se = qkv_se[:, 0].astype(jnp.float32)
    u_se = (qkv_se[:, 1].astype(jnp.float32) * qkv_se[:, 2].astype(jnp.float32)).astype(
        jnp.bfloat16
    )
    incoming_se = shifted(u_se[row_count - (SE_TAPS - 1) :], "seq", 1)
    extended = jnp.concatenate([incoming_se, u_se], axis=0).astype(jnp.float32)
    per_channel = jnp.repeat(taps_se.astype(jnp.float32), GROUP, axis=0)
    conv_se = jnp.zeros((row_count, chan_width), jnp.float32)
    for tap_index in range(SE_TAPS):
        begin = SE_TAPS - 1 - tap_index
        conv_se = conv_se + per_channel[:, tap_index] * extended[begin : begin + row_count]
    y_se = (query_se * (conv_se + skip_se.astype(jnp.float32) * u_se.astype(jnp.float32))).astype(
        jnp.bfloat16
    )
    gain_full = norm_gain.astype(jnp.float32)
    partial_out = project_out(y_se, w_out)
    share = lax.psum_scatter(partial_out, "tp", scatter_dimension=1, tiled=True)[:, 0]
    w_in_after, _ = lax.optimization_barrier((w_in, partial_out))
    w_full = absolute_rows(gather_rows(w_in_after))
    share, w_full = lax.optimization_barrier((share, w_full))
    stream = residual.astype(jnp.float32) + share
    squares = tp_sum(jnp.sum(stream * stream, axis=1))
    scale = lax.rsqrt(squares / (chan_width * lax.axis_size("tp")) + norm_eps)
    my_gain = lax.dynamic_slice_in_dim(gain_full, lax.axis_index("tp") * chan_width, chan_width, 0)
    normed = (stream * scale[:, None] * my_gain).astype(jnp.bfloat16)
    gathered = tp_gather(normed)
    weights = w_full.reshape(gathered.shape[0], gathered.shape[2], *w_in.shape[1:])
    proj = jnp.einsum("ktf,kfin->tin", gathered, weights, preferred_element_type=jnp.float32)
    query_mr = proj[:, 0]
    u_mr = (proj[:, 1] * proj[:, 2]).astype(jnp.bfloat16)
    lower, upper = toeplitz_pair(taps_mr)
    block_count = row_count // MR_TAPS
    blocks = u_mr.reshape(block_count, MR_TAPS, local_groups, GROUP)
    inside = jnp.einsum("gts,bsgc->btgc", lower, blocks, preferred_element_type=jnp.float32)
    tail_rows = shifted(blocks[block_count - 1], "seq", 1)
    earlier = jnp.concatenate([tail_rows[None], blocks[: block_count - 1]], axis=0)
    conv_mr = inside + jnp.einsum(
        "gts,bsgc->btgc", upper, earlier, preferred_element_type=jnp.float32
    )
    conv_mr = conv_mr.reshape(row_count, chan_width)
    return (query_mr * (conv_mr + skip_mr.astype(jnp.float32) * u_mr.astype(jnp.float32))).astype(
        jnp.bfloat16
    )


def solution(mesh):
    placed = (
        P("seq", None, "tp"),
        P("seq", "tp"),
        P("tp", None),
        P("tp"),
        P("tp", "seq"),
        P(),
        P("seq", None, "tp"),
        P("tp", None),
        P("tp"),
    )
    return jax.shard_map(
        per_device, mesh=mesh, in_specs=placed, out_specs=P("seq", "tp"), check_vma=False
    )
```

```python
import jax
import jax.numpy as jnp
from jax import lax
from jax.sharding import PartitionSpec as P

GROUP = 16
SE_TAPS = 7
MR_TAPS = 128


norm_eps = 1e-05


def shifted(block, axis, distance):
    devices = range(lax.axis_size(axis))
    route = [(i - distance, i) for i in devices if i - distance in devices]
    return lax.ppermute(block, axis, route)


def seq_coords(index):
    return index // 4, (index // 2) % 2, index % 2


def seq_of(z, y_lo, core):
    return z * 4 + y_lo * 2 + core


def exchange(block, axis, pairs):
    return lax.ppermute(block, axis, pairs)


def gather_rows(piece):
    seq_size = lax.axis_size("seq")
    z_size = seq_size // 4
    me = lax.axis_index("seq")
    other = exchange(piece, "seq", [(i, i ^ 2) for i in range(seq_size)])
    mine_first = (me // 2) % 2 == 0
    block = jnp.stack(
        [jnp.where(mine_first, piece, other), jnp.where(mine_first, other, piece)]
    )
    ahead = []
    behind = []
    for i in range(seq_size):
        z, y_lo, core = seq_coords(i)
        ahead.append((i, seq_of((z + 1) % z_size, y_lo, core)))
        behind.append((i, seq_of((z - 1) % z_size, y_lo, core)))
    core_pair = [(i, i ^ 1) for i in range(seq_size)]
    blocks = [(0, block)]
    moving_up = block
    moving_down = block
    for step in range(1, z_size // 2 + 1):
        moving_up = exchange(moving_up, "seq", ahead)
        blocks.append((step, moving_up))
        if step < z_size // 2:
            moving_down = exchange(moving_down, "seq", behind)
            blocks.append((z_size - step, moving_down))
    return [(k, mine, exchange(mine, "seq", core_pair)) for k, mine in blocks]


def absolute_rows(pieces):
    me = lax.axis_index("seq")
    my_z = me // 4
    mine_first = me % 2 == 0
    by_offset = jnp.stack(
        [
            jnp.where(
                mine_first, jnp.stack([mine, partner], axis=1), jnp.stack([partner, mine], axis=1)
            )
            for _, mine, partner in sorted(pieces)
        ]
    )
    z_size = by_offset.shape[0]
    reverse = by_offset[::-1]
    doubled = jnp.concatenate([reverse, reverse], axis=0)
    return lax.dynamic_slice_in_dim(doubled, (z_size - 1 - my_z) % z_size, z_size, axis=0)


def tp_sum(value):
    tp_size = lax.axis_size("tp")
    total = value
    bit = 1
    while bit < tp_size:
        total = total + lax.ppermute(total, "tp", [(i, i ^ bit) for i in range(tp_size)])
        bit *= 2
    return total


def tp_gather(block):
    tp_size = lax.axis_size("tp")
    x_size = tp_size // 2
    me = lax.axis_index("tp")
    my_x = me % x_size
    y_first = me // x_size == 0
    other = lax.ppermute(block, "tp", [(i, i ^ x_size) for i in range(tp_size)])
    pair = jnp.stack([jnp.where(y_first, block, other), jnp.where(y_first, other, block)])
    up = [(i, (i // x_size) * x_size + (i % x_size + 1) % x_size) for i in range(tp_size)]
    down = [(i, (i // x_size) * x_size + (i % x_size - 1) % x_size) for i in range(tp_size)]
    from_below = lax.ppermute(pair, "tp", up)
    from_above = lax.ppermute(pair, "tp", down)
    from_far = lax.ppermute(from_below, "tp", up)
    by_offset = jnp.stack([pair, from_above, from_far, from_below])
    doubled = jnp.concatenate([by_offset, by_offset], axis=0)
    by_x = lax.dynamic_slice_in_dim(doubled, (x_size - my_x) % x_size, x_size, axis=0)
    return jnp.swapaxes(by_x, 0, 1).reshape(tp_size, *block.shape)


def toeplitz_pair(taps):
    offsets = lax.broadcasted_iota(jnp.int32, (MR_TAPS, MR_TAPS), 0) - lax.broadcasted_iota(
        jnp.int32, (MR_TAPS, MR_TAPS), 1
    )
    lag_ids = lax.broadcasted_iota(jnp.int32, (MR_TAPS, MR_TAPS, MR_TAPS), 0)
    picks = (jnp.remainder(offsets, MR_TAPS)[None] == lag_ids).astype(jnp.bfloat16)
    table = jnp.einsum("gj,jts->gts", taps, picks, preferred_element_type=jnp.float32).astype(
        jnp.bfloat16
    )
    lower = jnp.where(offsets[None] >= 0, table, jnp.zeros_like(table))
    upper = jnp.where(offsets[None] < 0, table, jnp.zeros_like(table))
    return (lower, upper)


def project_out(y_se, w_out):
    by_z = absolute_rows(gather_rows(w_out))
    partial = jnp.einsum("tc,zyxcf->tzyxf", y_se, by_z, preferred_element_type=jnp.float32)
    return partial.reshape(y_se.shape[0], by_z.shape[0], -1)


def per_device(qkv_se, residual, taps_se, skip_se, w_out, norm_gain, w_in, taps_mr, skip_mr):
    row_count = qkv_se.shape[0]
    chan_width = qkv_se.shape[2]
    local_groups = chan_width // GROUP
    query_se = qkv_se[:, 0].astype(jnp.float32)
    u_se = (qkv_se[:, 1].astype(jnp.float32) * qkv_se[:, 2].astype(jnp.float32)).astype(
        jnp.bfloat16
    )
    incoming_se = shifted(u_se[row_count - (SE_TAPS - 1) :], "seq", 1)
    extended = jnp.concatenate([incoming_se, u_se], axis=0).astype(jnp.float32)
    per_channel = jnp.repeat(taps_se.astype(jnp.float32), GROUP, axis=0)
    conv_se = jnp.zeros((row_count, chan_width), jnp.float32)
    for tap_index in range(SE_TAPS):
        begin = SE_TAPS - 1 - tap_index
        conv_se = conv_se + per_channel[:, tap_index] * extended[begin : begin + row_count]
    y_se = (query_se * (conv_se + skip_se.astype(jnp.float32) * u_se.astype(jnp.float32))).astype(
        jnp.bfloat16
    )
    gain_full = norm_gain.astype(jnp.float32)
    partial_out = project_out(y_se, w_out)
    share = lax.psum_scatter(partial_out, "tp", scatter_dimension=1, tiled=True)[:, 0]
    w_in_after, _ = lax.optimization_barrier((w_in, partial_out))
    w_full = absolute_rows(gather_rows(w_in_after))
    share, w_full = lax.optimization_barrier((share, w_full))
    stream = residual.astype(jnp.float32) + share
    squares = tp_sum(jnp.sum(stream * stream, axis=1))
    scale = lax.rsqrt(squares / (chan_width * lax.axis_size("tp")) + norm_eps)
    my_gain = lax.dynamic_slice_in_dim(gain_full, lax.axis_index("tp") * chan_width, chan_width, 0)
    unscaled = (stream * my_gain).astype(jnp.bfloat16)
    gathered = tp_gather(unscaled)
    weights = w_full.reshape(gathered.shape[0], gathered.shape[2], *w_in.shape[1:])
    proj = (
        jnp.einsum("ktf,kfin->tin", gathered, weights, preferred_element_type=jnp.float32)
        * scale[:, None, None]
    )
    query_mr = proj[:, 0]
    u_mr = (proj[:, 1] * proj[:, 2]).astype(jnp.bfloat16)
    lower, upper = toeplitz_pair(taps_mr)
    block_count = row_count // MR_TAPS
    blocks = u_mr.reshape(block_count, MR_TAPS, local_groups, GROUP)
    inside = jnp.einsum("gts,bsgc->btgc", lower, blocks, preferred_element_type=jnp.float32)
    tail_rows = shifted(blocks[block_count - 1], "seq", 1)
    earlier = jnp.concatenate([tail_rows[None], blocks[: block_count - 1]], axis=0)
    conv_mr = inside + jnp.einsum(
        "gts,bsgc->btgc", upper, earlier, preferred_element_type=jnp.float32
    )
    conv_mr = conv_mr.reshape(row_count, chan_width)
    return (query_mr * (conv_mr + skip_mr.astype(jnp.float32) * u_mr.astype(jnp.float32))).astype(
        jnp.bfloat16
    )


def solution(mesh):
    placed = (
        P("seq", None, "tp"),
        P("seq", "tp"),
        P("tp", None),
        P("tp"),
        P("tp", "seq"),
        P(),
        P("seq", None, "tp"),
        P("tp", None),
        P("tp"),
    )
    return jax.shard_map(
        per_device, mesh=mesh, in_specs=placed, out_specs=P("seq", "tp"), check_vma=False
    )
```

```python
import jax
import jax.numpy as jnp
from jax import lax
from jax.sharding import PartitionSpec as P

GROUP = 16
SE_TAPS = 7
MR_TAPS = 128


norm_eps = 1e-05


def shifted(block, axis, distance):
    devices = range(lax.axis_size(axis))
    route = [(i - distance, i) for i in devices if i - distance in devices]
    return lax.ppermute(block, axis, route)


def seq_coords(index):
    return index // 4, (index // 2) % 2, index % 2


def seq_of(z, y_lo, core):
    return z * 4 + y_lo * 2 + core


def exchange(block, axis, pairs):
    return lax.ppermute(block, axis, pairs)


def gather_rows(piece):
    seq_size = lax.axis_size("seq")
    z_size = seq_size // 4
    me = lax.axis_index("seq")
    other = exchange(piece, "seq", [(i, i ^ 2) for i in range(seq_size)])
    mine_first = (me // 2) % 2 == 0
    block = jnp.stack(
        [jnp.where(mine_first, piece, other), jnp.where(mine_first, other, piece)]
    )
    ahead = []
    behind = []
    for i in range(seq_size):
        z, y_lo, core = seq_coords(i)
        ahead.append((i, seq_of((z + 1) % z_size, y_lo, core)))
        behind.append((i, seq_of((z - 1) % z_size, y_lo, core)))
    core_pair = [(i, i ^ 1) for i in range(seq_size)]
    blocks = [(0, block)]
    moving_up = block
    moving_down = block
    for step in range(1, z_size // 2 + 1):
        moving_up = exchange(moving_up, "seq", ahead)
        blocks.append((step, moving_up))
        if step < z_size // 2:
            moving_down = exchange(moving_down, "seq", behind)
            blocks.append((z_size - step, moving_down))
    return [(k, mine, exchange(mine, "seq", core_pair)) for k, mine in blocks]


def absolute_rows(pieces):
    me = lax.axis_index("seq")
    my_z = me // 4
    mine_first = me % 2 == 0
    by_offset = jnp.stack(
        [
            jnp.where(
                mine_first, jnp.stack([mine, partner], axis=1), jnp.stack([partner, mine], axis=1)
            )
            for _, mine, partner in sorted(pieces)
        ]
    )
    z_size = by_offset.shape[0]
    reverse = by_offset[::-1]
    doubled = jnp.concatenate([reverse, reverse], axis=0)
    return lax.dynamic_slice_in_dim(doubled, (z_size - 1 - my_z) % z_size, z_size, axis=0)


def tp_sum(value):
    tp_size = lax.axis_size("tp")
    total = value
    bit = 1
    while bit < tp_size:
        total = total + lax.ppermute(total, "tp", [(i, i ^ bit) for i in range(tp_size)])
        bit *= 2
    return total


def tp_gather(block):
    tp_size = lax.axis_size("tp")
    x_size = tp_size // 2
    me = lax.axis_index("tp")
    my_x = me % x_size
    y_first = me // x_size == 0
    other = lax.ppermute(block, "tp", [(i, i ^ x_size) for i in range(tp_size)])
    pair = jnp.stack([jnp.where(y_first, block, other), jnp.where(y_first, other, block)])
    up = [(i, (i // x_size) * x_size + (i % x_size + 1) % x_size) for i in range(tp_size)]
    down = [(i, (i // x_size) * x_size + (i % x_size - 1) % x_size) for i in range(tp_size)]
    from_below = lax.ppermute(pair, "tp", up)
    from_above = lax.ppermute(pair, "tp", down)
    from_far = lax.ppermute(from_below, "tp", up)
    by_offset = jnp.stack([pair, from_above, from_far, from_below])
    doubled = jnp.concatenate([by_offset, by_offset], axis=0)
    by_x = lax.dynamic_slice_in_dim(doubled, (x_size - my_x) % x_size, x_size, axis=0)
    return jnp.swapaxes(by_x, 0, 1).reshape(tp_size, *block.shape)


def toeplitz_pair(taps):
    offsets = lax.broadcasted_iota(jnp.int32, (MR_TAPS, MR_TAPS), 0) - lax.broadcasted_iota(
        jnp.int32, (MR_TAPS, MR_TAPS), 1
    )
    lag_ids = lax.broadcasted_iota(jnp.int32, (MR_TAPS, MR_TAPS, MR_TAPS), 0)
    picks = (jnp.remainder(offsets, MR_TAPS)[None] == lag_ids).astype(jnp.bfloat16)
    table = jnp.einsum("gj,jts->gts", taps, picks, preferred_element_type=jnp.float32).astype(
        jnp.bfloat16
    )
    lower = jnp.where(offsets[None] >= 0, table, jnp.zeros_like(table))
    upper = jnp.where(offsets[None] < 0, table, jnp.zeros_like(table))
    return (lower, upper)


def project_out(y_se, w_out):
    by_z = absolute_rows(gather_rows(w_out))
    partial = jnp.einsum("tc,zyxcf->tzyxf", y_se, by_z, preferred_element_type=jnp.float32)
    return partial.reshape(y_se.shape[0], by_z.shape[0], -1)


def per_device(qkv_se, residual, taps_se, skip_se, w_out, norm_gain, w_in, taps_mr, skip_mr):
    row_count = qkv_se.shape[0]
    chan_width = qkv_se.shape[2]
    local_groups = chan_width // GROUP
    query_se = qkv_se[:, 0].astype(jnp.float32)
    u_se = (qkv_se[:, 1].astype(jnp.float32) * qkv_se[:, 2].astype(jnp.float32)).astype(
        jnp.bfloat16
    )
    incoming_se = shifted(u_se[row_count - (SE_TAPS - 1) :], "seq", 1)
    extended = jnp.concatenate([incoming_se, u_se], axis=0).astype(jnp.float32)
    per_channel = jnp.repeat(taps_se.astype(jnp.float32), GROUP, axis=0)
    conv_se = jnp.zeros((row_count, chan_width), jnp.float32)
    for tap_index in range(SE_TAPS):
        begin = SE_TAPS - 1 - tap_index
        conv_se = conv_se + per_channel[:, tap_index] * extended[begin : begin + row_count]
    y_se = (query_se * (conv_se + skip_se.astype(jnp.float32) * u_se.astype(jnp.float32))).astype(
        jnp.bfloat16
    )
    gain_full = norm_gain.astype(jnp.float32)
    partial_out = project_out(y_se, w_out)
    share = lax.psum_scatter(partial_out, "tp", scatter_dimension=1, tiled=True)[:, 0]
    w_in_after, _ = lax.optimization_barrier((w_in, partial_out))
    w_full = absolute_rows(gather_rows(w_in_after))
    share, w_full = lax.optimization_barrier((share, w_full))
    stream = residual.astype(jnp.float32) + share
    squares = tp_sum(jnp.sum(stream * stream, axis=1))
    scale = lax.rsqrt(squares / (chan_width * lax.axis_size("tp")) + norm_eps)
    my_gain = lax.dynamic_slice_in_dim(gain_full, lax.axis_index("tp") * chan_width, chan_width, 0)
    normed = (stream * scale[:, None] * my_gain).astype(jnp.bfloat16)
    gathered = tp_gather(normed)
    weights = w_full.reshape(gathered.shape[0], gathered.shape[2], *w_in.shape[1:])
    proj = jnp.einsum("ktf,kfin->tin", gathered, weights, preferred_element_type=jnp.float32)
    query_mr = proj[:, 0]
    u_mr = (proj[:, 1] * proj[:, 2]).astype(jnp.bfloat16)
    lower, upper = toeplitz_pair(taps_mr)
    block_count = row_count // MR_TAPS
    blocks = u_mr.reshape(block_count, MR_TAPS, local_groups, GROUP)
    inside = jnp.einsum("gts,bsgc->btgc", lower, blocks, preferred_element_type=jnp.float32)
    tail_rows = shifted(blocks[block_count - 1], "seq", 1)
    earlier = jnp.concatenate([tail_rows[None], blocks[: block_count - 1]], axis=0)
    conv_mr = inside + jnp.einsum(
        "gts,bsgc->btgc", upper, earlier, preferred_element_type=jnp.float32
    )
    conv_mr = conv_mr.reshape(row_count, chan_width)
    return (query_mr * (conv_mr + skip_mr.astype(jnp.float32) * u_mr.astype(jnp.float32))).astype(
        jnp.bfloat16
    )


def solution(mesh):
    placed = (
        P("seq", None, "tp"),
        P("seq", "tp"),
        P("tp", None),
        P("tp"),
        P("tp", "seq"),
        P(),
        P("seq", None, "tp"),
        P("tp", None),
        P("tp"),
    )
    return jax.shard_map(
        per_device, mesh=mesh, in_specs=placed, out_specs=P("seq", "tp"), check_vma=False
    )
```
